512 devices in a mesh: row: 16 (over z_hi, x), col: 32 (over y, z_lo, core).
Axes of the slice: x: 4, y: 8, z: 8 (z_hi: 4, z_lo: 2; z = z_hi * 2 + z_lo), core: 2. Of those that a mesh axis runs over, the one named last changes fastest.
Arguments:
- slab: float32 [16384, 16384], P('row', 'col'), may hold values from -3 to 3
- u_codes: bfloat16 [2, 32, 512, 384], P(None, 'row', 'col'), may hold values from -0.8984375 to 0.8984375
- v_codes: bfloat16 [2, 32, 1024, 384], P(None, 'row', 'col'), may hold values from -0.1875 to 0.1875
- u_scale: float32 [2, 32, 384], replicated, may hold values from 0.5 to 2.5
- v_scale: float32 [2, 32, 384], replicated, may hold values from 0.5 to 2.5
- ranks: int32 [2, 32], replicated, may hold values from 64 to 384, as said below
- d_inverse: float32 [2, 2, 2, 512], replicated, may hold values from -0.6 to 2, as said below
Outputs:
- updated: float32 [16384, 16384], P('row', 'col')
The draws below stay inside these ranges and needn't reach their ends.
Inputs may be any that keep to these rules, and one draw needn't show every extreme that they name: `ranks`: every rank is one of 64, 128, 256 and 384; every panel has a tile of rank 384. `d_inverse`: each 2 x 2 block is symmetric positive definite, its diagonal entries between 0.5 and 2, its off-diagonal entry under 0.3 times the root of their product in magnitude.
All inputs are finite; a program needn't handle non-finite values.
Results may differ from the reference program's by a relative error of at most 0.0042.
Values may be sent and summed in bfloat16 or wider, within the bound.
No kernel may reach another device: no remote copies, remote signals or barrier semaphores. Data moves between devices by JAX's collectives and lax.ppermute only.
A program may use at most 128 MiB of HBM per device.

```python
import math
import jax
import jax.numpy as jnp
from jax import lax

TS = 512
B = 1024
R = 384
K = 2
TILES = 32
ORDER = 16384


def draw_ranks(key, part):
    first_key = jax.random.fold_in(key, 11)
    second_key = jax.random.fold_in(key, 23)
    bucket = jax.random.randint(first_key, (K, TILES), 0, 4)
    heavy = jax.random.randint(second_key, (K, 1), 0, TILES)
    position = jnp.arange(TILES, dtype=jnp.int32)[None, :]
    bucket = jnp.where(position == heavy, 3, bucket)
    table = jnp.array([1, 2, 4, 6], dtype=jnp.int32)
    return (R // 6 * table[bucket]).astype(jnp.int32)


def draw_d_inverse(key, part):
    shape = (K, B // 2)
    key_a = jax.random.fold_in(key, 5)
    key_b = jax.random.fold_in(key, 7)
    key_c = jax.random.fold_in(key, 9)
    diag_first = jax.random.uniform(key_a, shape, jnp.float32, 0.5, 2.0)
    diag_second = jax.random.uniform(key_b, shape, jnp.float32, 0.5, 2.0)
    tilt = jax.random.uniform(key_c, shape, jnp.float32, -0.99, 0.99)
    off = 0.3 * jnp.sqrt(diag_first * diag_second) * tilt
    blocks = jnp.stack([jnp.stack([diag_first, off]), jnp.stack([off, diag_second])])
    return jnp.transpose(blocks, (2, 0, 1, 3)).astype(jnp.float32)


def shard_levels(key, shape, pieces, low, largest):
    def one(dim, blocks):
        steps = jax.random.uniform(jax.random.fold_in(jax.random.fold_in(key, 6), dim), (blocks,), jnp.float32, low / len(pieces), largest / len(pieces))
        return jnp.repeat(jnp.exp(steps), shape[dim] // blocks).reshape((-1,) + (1,) * (len(shape) - dim - 1))

    factor_of = one(*pieces[0])
    for cut in pieces[1:]:
        factor_of = factor_of * one(*cut)
    return factor_of


def gaussian(key, extent, width, most, cuts=(), kind=jnp.bfloat16):
    factor_of = shard_levels(key, extent, cuts, -0.22, 0.18) if cuts else 1.0
    entries = jax.random.normal(key, extent, jnp.float32) * width * factor_of
    return jnp.minimum(jnp.maximum(entries, -most), most).astype(kind)


def setup_inputs(seed: int = 0) -> dict:
    arg_keys = jax.random.split(jax.random.key(seed), 8)
    return {
        "slab": gaussian(arg_keys[0], (ORDER, ORDER), 0.5, 3.0, ((0, 16), (1, 32)), jnp.float32),
        "u_codes": gaussian(arg_keys[1], (K, TILES, TS, R), 0.15, 0.8984375, ((1, 16), (2, 32))),
        "v_codes": gaussian(arg_keys[2], (K, TILES, B, R), B ** -0.5, 0.1875, ((1, 16), (2, 32))),
        "u_scale": jnp.clip(jnp.exp(jax.random.uniform(arg_keys[3], (K, TILES, R), jnp.float32, math.log(0.5), math.log(2.5))), 0.5, 2.5),
        "v_scale": jnp.clip(jnp.exp(jax.random.uniform(arg_keys[4], (K, TILES, R), jnp.float32, math.log(0.5), math.log(2.5))), 0.5, 2.5),
        "ranks": draw_ranks(jax.random.fold_in(arg_keys[7], 71), 0),
        "d_inverse": draw_d_inverse(jax.random.fold_in(arg_keys[7], 71), 0),
    }


def column_weight(u_scale_k, v_scale_k, ranks_k):
    position = lax.broadcasted_iota(jnp.int32, u_scale_k.shape, 1)
    return jnp.where(position < ranks_k[:, None], u_scale_k * v_scale_k, jnp.float32(0.0))


def apply_inverse(d_block, codes):
    shape = codes.shape
    pairs = codes.reshape(shape[:-2] + (shape[-2] // 2, 2, shape[-1]))
    even = pairs[..., 0, :].astype(jnp.float32)
    odd = pairs[..., 1, :].astype(jnp.float32)
    first = d_block[0, 0][:, None] * even + d_block[0, 1][:, None] * odd
    second = d_block[1, 0][:, None] * even + d_block[1, 1][:, None] * odd
    return jnp.stack([first, second], axis=-2).reshape(shape).astype(jnp.bfloat16)


def reference(slab, u_codes, v_codes, u_scale, v_scale, ranks, d_inverse):
    panels = u_codes.shape[0]
    tiles = u_codes.shape[1]
    tile_order = u_codes.shape[2]
    weights = [column_weight(u_scale[k], v_scale[k], ranks[k]) for k in range(panels)]
    scaled = [apply_inverse(d_inverse[k], v_codes[k]).astype(jnp.float32) for k in range(panels)]
    left_all = [u_codes[k].astype(jnp.float32) for k in range(panels)]
    right_all = [v_codes[k].astype(jnp.float32) for k in range(panels)]
    rows = slab.reshape(tiles, tile_order, tiles * tile_order)

    def one_row(items):
        block, index = items
        for k in range(panels):
            cv_row = right_all[k][index]
            weight_row = weights[k][index]
            inner = jnp.einsum("br,tbq->rtq", cv_row, scaled[k])
            core = (weight_row[:, None, None] * inner * weights[k][None, :, :]).astype(jnp.bfloat16)
            left = jnp.einsum("mr,rtq->mtq", left_all[k][index], core.astype(jnp.float32)).astype(jnp.bfloat16)
            update = jnp.einsum("mtq,tnq->mtn", left.astype(jnp.float32), left_all[k])
            block = block - update.reshape(tile_order, tiles * tile_order)
        return block

    result = lax.map(one_row, (rows, jnp.arange(tiles, dtype=jnp.int32)))
    return result.reshape(slab.shape)
```

```python
import jax
import jax.numpy as jnp
from jax import lax
from jax.sharding import PartitionSpec as P


def column_weight(u_scale_k, v_scale_k, ranks_k):
    position = lax.broadcasted_iota(jnp.int32, u_scale_k.shape, 1)
    return jnp.where(position < ranks_k[:, None], u_scale_k * v_scale_k, jnp.float32(0.0))


def apply_inverse(d_block, codes):
    shape = codes.shape
    pairs = codes.reshape(shape[:-2] + (shape[-2] // 2, 2, shape[-1]))
    even = pairs[..., 0, :].astype(jnp.float32)
    odd = pairs[..., 1, :].astype(jnp.float32)
    first = d_block[0, 0][:, None] * even + d_block[0, 1][:, None] * odd
    second = d_block[1, 0][:, None] * even + d_block[1, 1][:, None] * odd
    return jnp.stack([first, second], axis=-2).reshape(shape).astype(jnp.bfloat16)


def local(slab, u_codes, v_codes, u_scale, v_scale, ranks, d_inverse):
    panels, per_row, u_rows, rank_most = u_codes.shape
    v_rows = v_codes.shape[2]
    n_col = lax.axis_size("col")
    column = lax.axis_index("col")
    first_tile = lax.axis_index("row") * per_row
    both = u_rows + v_rows

    shard = jnp.concatenate([u_codes, v_codes], axis=2)

    row_all = lax.all_gather(shard, "col", axis=2, tiled=True)
    row_all = row_all.reshape(panels, per_row, n_col, both, rank_most)
    row_u = row_all[:, :, :, :u_rows].reshape(panels, per_row, n_col * u_rows, rank_most)
    row_v = row_all[:, :, :, u_rows:].reshape(panels, per_row, n_col * v_rows, rank_most)

    every_tile = lax.all_gather(shard, "row", axis=1, tiled=True)
    col_all = lax.all_to_all(every_tile, "col", 1, 2, tiled=True)
    col_all = col_all.reshape(panels, n_col, both, rank_most)
    col_u = col_all[:, :, :u_rows].reshape(panels, n_col * u_rows, rank_most)
    col_v = col_all[:, :, u_rows:].reshape(panels, n_col * v_rows, rank_most)

    weight = jnp.stack(
        [column_weight(u_scale[k], v_scale[k], ranks[k]) for k in range(panels)]
    )
    row_weight = lax.dynamic_slice_in_dim(weight, first_tile, per_row, 1)
    col_weight = lax.dynamic_index_in_dim(weight, column, 1, keepdims=False)
    col_scaled = jnp.stack([apply_inverse(d_inverse[k], col_v[k]) for k in range(panels)])

    inner = jnp.einsum("kibr,kbq->kirq", row_v, col_scaled, preferred_element_type=jnp.float32)
    core = (row_weight[:, :, :, None] * inner * col_weight[:, None, None, :]).astype(jnp.bfloat16)
    left = jnp.einsum("kimr,kirq->kimq", row_u, core, preferred_element_type=jnp.float32)
    left = left.astype(jnp.bfloat16)
    update = jnp.einsum("kimq,knq->imn", left, col_u, preferred_element_type=jnp.float32)
    return slab - update.reshape(slab.shape)


def solution(mesh):
    in_specs = (
        P("row", "col"),
        P(None, "row", "col", None),
        P(None, "row", "col", None),
        P(),
        P(),
        P(),
        P(),
    )
    out_specs = P("row", "col")
    return jax.shard_map(local, mesh=mesh, in_specs=in_specs, out_specs=out_specs, check_vma=False)
```

```python
import jax
import jax.numpy as jnp
from jax import lax
from jax.sharding import PartitionSpec as P


def column_weight(u_scale_k, v_scale_k, ranks_k):
    position = lax.broadcasted_iota(jnp.int32, u_scale_k.shape, 1)
    return jnp.where(position < ranks_k[:, None], u_scale_k * v_scale_k, jnp.float32(0.0))


def local(slab, u_codes, v_codes, u_scale, v_scale, ranks, d_inverse):
    panels, per_row, u_rows, rank_most = u_codes.shape
    v_rows = v_codes.shape[2]
    n_col = lax.axis_size("col")
    column = lax.axis_index("col")
    first_tile = lax.axis_index("row") * per_row
    tile_order = n_col * u_rows

    shard = jnp.concatenate([u_codes, v_codes], axis=2).transpose(1, 0, 2, 3)

    row_all = lax.all_gather(shard, "col", axis=0, tiled=False)
    row_u = row_all[:, :, :, :u_rows]
    row_v = row_all[:, :, :, u_rows:]

    every_tile = lax.all_gather(shard, "row", axis=0, tiled=True)
    col_all = lax.all_to_all(every_tile, "col", 0, 0, tiled=True)
    col_u = col_all[:, :, :u_rows].transpose(1, 0, 2, 3).reshape(panels, tile_order, rank_most)
    col_v = col_all[:, :, u_rows:]

    weight = jnp.stack(
        [column_weight(u_scale[k], v_scale[k], ranks[k]) for k in range(panels)]
    )
    row_weight = lax.dynamic_slice_in_dim(weight, first_tile, per_row, 1)
    col_weight = lax.dynamic_index_in_dim(weight, column, 1, keepdims=False)

    half = v_rows // 2
    d_blocks = d_inverse.reshape(panels, 2, 2, n_col, half).transpose(1, 2, 3, 0, 4)[..., None]
    pairs = col_v.reshape(n_col, panels, half, 2, rank_most)
    even = pairs[..., 0, :].astype(jnp.float32)
    odd = pairs[..., 1, :].astype(jnp.float32)
    first = d_blocks[0, 0] * even + d_blocks[0, 1] * odd
    second = d_blocks[1, 0] * even + d_blocks[1, 1] * odd
    col_scaled = jnp.stack([first, second], axis=-2).reshape(col_v.shape).astype(jnp.bfloat16)

    inner = jnp.einsum("cikbr,ckbq->kirq", row_v, col_scaled, preferred_element_type=jnp.float32)
    core = (row_weight[:, :, :, None] * inner * col_weight[:, None, None, :]).astype(jnp.bfloat16)
    left = jnp.einsum("cikmr,kirq->kicmq", row_u, core, preferred_element_type=jnp.float32)
    left = left.astype(jnp.bfloat16)
    update = jnp.einsum("kicmq,knq->icmn", left, col_u, preferred_element_type=jnp.float32)
    return slab - update.reshape(slab.shape)


def solution(mesh):
    in_specs = (
        P("row", "col"),
        P(None, "row", "col", None),
        P(None, "row", "col", None),
        P(),
        P(),
        P(),
        P(),
    )
    out_specs = P("row", "col")
    return jax.shard_map(local, mesh=mesh, in_specs=in_specs, out_specs=out_specs, check_vma=False)
```

```python
import jax
import jax.numpy as jnp
from jax import lax
from jax.sharding import PartitionSpec as P


def column_weight(u_scale_k, v_scale_k, ranks_k):
    position = lax.broadcasted_iota(jnp.int32, u_scale_k.shape, 1)
    return jnp.where(position < ranks_k[:, None], u_scale_k * v_scale_k, jnp.float32(0.0))


def local(slab, u_codes, v_codes, u_scale, v_scale, ranks, d_inverse):
    panels, per_row, u_rows, rank_most = u_codes.shape
    v_rows = v_codes.shape[2]
    n_col = lax.axis_size("col")
    column = lax.axis_index("col")
    first_tile = lax.axis_index("row") * per_row
    tile_order = n_col * u_rows

    shard = jnp.concatenate([u_codes, v_codes], axis=2).transpose(1, 0, 2, 3)

    row_all = lax.all_gather(shard, "col", axis=0, tiled=False)
    row_u = row_all[:, :, :, :u_rows]
    row_v = row_all[:, :, :, u_rows:]

    n_row = lax.axis_size("row")
    spread = jnp.broadcast_to(shard[None], (n_row,) + shard.shape)
    every_tile = lax.all_to_all(spread, "row", 0, 0, tiled=True)
    every_tile = every_tile.reshape((n_row * per_row,) + shard.shape[1:])
    col_all = lax.all_to_all(every_tile, "col", 0, 0, tiled=True)
    col_u = col_all[:, :, :u_rows].transpose(1, 0, 2, 3).reshape(panels, tile_order, rank_most)
    col_v = col_all[:, :, u_rows:]

    weight = jnp.stack(
        [column_weight(u_scale[k], v_scale[k], ranks[k]) for k in range(panels)]
    )
    row_weight = lax.dynamic_slice_in_dim(weight, first_tile, per_row, 1)
    col_weight = lax.dynamic_index_in_dim(weight, column, 1, keepdims=False)

    half = v_rows // 2
    d_blocks = d_inverse.reshape(panels, 2, 2, n_col, half).transpose(1, 2, 3, 0, 4)[..., None]
    pairs = col_v.reshape(n_col, panels, half, 2, rank_most)
    even = pairs[..., 0, :].astype(jnp.float32)
    odd = pairs[..., 1, :].astype(jnp.float32)
    first = d_blocks[0, 0] * even + d_blocks[0, 1] * odd
    second = d_blocks[1, 0] * even + d_blocks[1, 1] * odd
    col_scaled = jnp.stack([first, second], axis=-2).reshape(col_v.shape).astype(jnp.bfloat16)

    inner = jnp.einsum("cikbr,ckbq->kirq", row_v, col_scaled, preferred_element_type=jnp.float32)
    core = (row_weight[:, :, :, None] * inner * col_weight[:, None, None, :]).astype(jnp.bfloat16)
    left = jnp.einsum("cikmr,kirq->kicmq", row_u, core, preferred_element_type=jnp.float32)
    left = left.astype(jnp.bfloat16)
    update = jnp.einsum("kicmq,knq->icmn", left, col_u, preferred_element_type=jnp.float32)
    return slab - update.reshape(slab.shape)


def solution(mesh):
    in_specs = (
        P("row", "col"),
        P(None, "row", "col", None),
        P(None, "row", "col", None),
        P(),
        P(),
        P(),
        P(),
    )
    out_specs = P("row", "col")
    return jax.shard_map(local, mesh=mesh, in_specs=in_specs, out_specs=out_specs, check_vma=False)
```

```python
import jax
import jax.numpy as jnp
from jax import lax
from jax.sharding import Mesh, PartitionSpec as P


def column_weight(u_scale_k, v_scale_k, ranks_k):
    position = lax.broadcasted_iota(jnp.int32, u_scale_k.shape, 1)
    return jnp.where(position < ranks_k[:, None], u_scale_k * v_scale_k, jnp.float32(0.0))


def local(slab, u_codes, v_codes, u_scale, v_scale, ranks, d_inverse):
    panels, per_row, u_rows, rank_most = u_codes.shape
    v_rows = v_codes.shape[2]
    n_col = lax.axis_size("col")
    column = lax.axis_index("col")
    first_tile = (lax.axis_index("zh") * lax.axis_size("x") + lax.axis_index("x")) * per_row
    tile_order = n_col * u_rows

    shard = jnp.concatenate([u_codes, v_codes], axis=2).transpose(1, 0, 2, 3)

    row_all = lax.all_gather(shard, "col", axis=0, tiled=False)
    row_u = row_all[:, :, :, :u_rows]
    row_v = row_all[:, :, :, u_rows:]

    n_x = lax.axis_size("x")
    n_z = lax.axis_size("zh")
    spread = jnp.broadcast_to(shard[None], (n_x,) + shard.shape)
    by_x = lax.all_to_all(spread, "x", 0, 0, tiled=True)
    spread = jnp.broadcast_to(by_x[None], (n_z,) + by_x.shape)
    every_tile = lax.all_to_all(spread, "zh", 0, 0, tiled=True)
    every_tile = every_tile.reshape((n_z * n_x * per_row,) + shard.shape[1:])
    col_all = lax.all_to_all(every_tile, "col", 0, 0, tiled=True)
    col_u = col_all[:, :, :u_rows].transpose(1, 0, 2, 3).reshape(panels, tile_order, rank_most)
    col_v = col_all[:, :, u_rows:]

    weight = jnp.stack(
        [column_weight(u_scale[k], v_scale[k], ranks[k]) for k in range(panels)]
    )
    row_weight = lax.dynamic_slice_in_dim(weight, first_tile, per_row, 1)
    col_weight = lax.dynamic_index_in_dim(weight, column, 1, keepdims=False)

    half = v_rows // 2
    d_blocks = d_inverse.reshape(panels, 2, 2, n_col, half).transpose(1, 2, 3, 0, 4)[..., None]
    pairs = col_v.reshape(n_col, panels, half, 2, rank_most)
    even = pairs[..., 0, :].astype(jnp.float32)
    odd = pairs[..., 1, :].astype(jnp.float32)
    first = d_blocks[0, 0] * even + d_blocks[0, 1] * odd
    second = d_blocks[1, 0] * even + d_blocks[1, 1] * odd
    col_scaled = jnp.stack([first, second], axis=-2).reshape(col_v.shape).astype(jnp.bfloat16)

    inner = jnp.einsum("cikbr,ckbq->kirq", row_v, col_scaled, preferred_element_type=jnp.float32)
    core = (row_weight[:, :, :, None] * inner * col_weight[:, None, None, :]).astype(jnp.bfloat16)
    left = jnp.einsum("cikmr,kirq->kicmq", row_u, core, preferred_element_type=jnp.float32)
    left = left.astype(jnp.bfloat16)
    update = jnp.einsum("kicmq,knq->icmn", left, col_u, preferred_element_type=jnp.float32)
    return slab - update.reshape(slab.shape)


def solution(mesh):
    n_row, n_col = mesh.devices.shape
    n_x = 4 if n_row % 4 == 0 else 1
    split = Mesh(mesh.devices.reshape(n_row // n_x, n_x, n_col), ("zh", "x", "col"))
    rows = ("zh", "x")
    in_specs = (
        P(rows, "col"),
        P(None, rows, "col", None),
        P(None, rows, "col", None),
        P(),
        P(),
        P(),
        P(),
    )
    out_specs = P(rows, "col")
    return jax.shard_map(local, mesh=split, in_specs=in_specs, out_specs=out_specs, check_vma=False)
```

```python
import jax
import jax.numpy as jnp
from jax import lax
from jax.sharding import PartitionSpec as P


def column_weight(u_scale_k, v_scale_k, ranks_k):
    position = lax.broadcasted_iota(jnp.int32, u_scale_k.shape, 1)
    return jnp.where(position < ranks_k[:, None], u_scale_k * v_scale_k, jnp.float32(0.0))


def local(slab, u_codes, v_codes, u_scale, v_scale, ranks, d_inverse):
    panels, per_row, u_rows, rank_most = u_codes.shape
    v_rows = v_codes.shape[2]
    n_col = lax.axis_size("col")
    column = lax.axis_index("col")
    first_tile = lax.axis_index("row") * per_row
    tile_order = n_col * u_rows
    both = u_rows + v_rows

    shard = jnp.concatenate([u_codes, v_codes], axis=2).transpose(1, 0, 2, 3)

    row_all = lax.all_gather(shard, "col", axis=0, tiled=False)
    row_u = row_all[:, :, :, :u_rows]
    row_v = row_all[:, :, :, u_rows:]

    n_row = lax.axis_size("row")
    flat = shard.reshape(per_row * panels * both, rank_most)
    spread = jnp.broadcast_to(flat[None], (n_row,) + flat.shape)
    every_tile = lax.all_to_all(spread, "row", 0, 0, tiled=True)
    every_tile = every_tile.reshape(n_row * per_row, panels * both, rank_most)
    col_all = lax.all_to_all(every_tile, "col", 0, 0, tiled=True)
    col_all = col_all.reshape(n_col, panels, both, rank_most)
    col_u = col_all[:, :, :u_rows].transpose(1, 0, 2, 3).reshape(panels, tile_order, rank_most)
    col_v = col_all[:, :, u_rows:]

    weight = jnp.stack(
        [column_weight(u_scale[k], v_scale[k], ranks[k]) for k in range(panels)]
    )
    row_weight = lax.dynamic_slice_in_dim(weight, first_tile, per_row, 1)
    col_weight = lax.dynamic_index_in_dim(weight, column, 1, keepdims=False)

    half = v_rows // 2
    d_blocks = d_inverse.reshape(panels, 2, 2, n_col, half).transpose(1, 2, 3, 0, 4)[..., None]
    pairs = col_v.reshape(n_col, panels, half, 2, rank_most)
    even = pairs[..., 0, :].astype(jnp.float32)
    odd = pairs[..., 1, :].astype(jnp.float32)
    first = d_blocks[0, 0] * even + d_blocks[0, 1] * odd
    second = d_blocks[1, 0] * even + d_blocks[1, 1] * odd
    col_scaled = jnp.stack([first, second], axis=-2).reshape(col_v.shape).astype(jnp.bfloat16)

    inner = jnp.einsum("cikbr,ckbq->kirq", row_v, col_scaled, preferred_element_type=jnp.float32)
    core = (row_weight[:, :, :, None] * inner * col_weight[:, None, None, :]).astype(jnp.bfloat16)
    left = jnp.einsum("cikmr,kirq->kicmq", row_u, core, preferred_element_type=jnp.float32)
    left = left.astype(jnp.bfloat16)
    update = jnp.einsum("kicmq,knq->icmn", left, col_u, preferred_element_type=jnp.float32)
    return slab - update.reshape(slab.shape)


def solution(mesh):
    in_specs = (
        P("row", "col"),
        P(None, "row", "col", None),
        P(None, "row", "col", None),
        P(),
        P(),
        P(),
        P(),
    )
    out_specs = P("row", "col")
    return jax.shard_map(local, mesh=mesh, in_specs=in_specs, out_specs=out_specs, check_vma=False)
```

```python
import jax
import jax.numpy as jnp
from jax import lax
from jax.sharding import PartitionSpec as P


def column_weight(u_scale_k, v_scale_k, ranks_k):
    position = lax.broadcasted_iota(jnp.int32, u_scale_k.shape, 1)
    return jnp.where(position < ranks_k[:, None], u_scale_k * v_scale_k, jnp.float32(0.0))


def ring_gather(block, n_outer, n_inner, outer):
    n = n_outer if outer else n_inner

    def target(r, step):
        a, b = divmod(r, n_inner)
        if outer:
            return ((a + step) % n_outer) * n_inner + b
        return a * n_inner + (b + step) % n_inner

    pieces = [block]
    for d in range(1, n):
        perm = [(r, target(r, -d)) for r in range(n_outer * n_inner)]
        pieces.append(lax.ppermute(block, "row", perm))
    return jnp.stack(pieces)


def replicate_over_row(block, n_row):
    n_x = 4 if n_row % 4 == 0 else n_row
    n_z = n_row // n_x
    row = lax.axis_index("row")
    z, x = row // n_x, row % n_x
    by_x = ring_gather(block, n_z, n_x, outer=False)
    by_zx = ring_gather(by_x, n_z, n_x, outer=True)
    by_zx = jnp.roll(jnp.roll(by_zx, z, axis=0), x, axis=1)
    return by_zx.reshape((n_row,) + block.shape)


def local(slab, u_codes, v_codes, u_scale, v_scale, ranks, d_inverse):
    panels, per_row, u_rows, rank_most = u_codes.shape
    v_rows = v_codes.shape[2]
    n_col = lax.axis_size("col")
    column = lax.axis_index("col")
    first_tile = lax.axis_index("row") * per_row
    tile_order = n_col * u_rows
    both = u_rows + v_rows

    shard = jnp.concatenate([u_codes, v_codes], axis=2).transpose(1, 0, 2, 3)

    row_all = lax.all_gather(shard, "col", axis=0, tiled=False)
    row_u = row_all[:, :, :, :u_rows]
    row_v = row_all[:, :, :, u_rows:]

    n_row = lax.axis_size("row")
    flat = shard.reshape(per_row * panels * both, rank_most)
    every_tile = replicate_over_row(flat, n_row)
    every_tile = every_tile.reshape(n_row * per_row, panels * both, rank_most)
    col_all = lax.all_to_all(every_tile, "col", 0, 0, tiled=True)
    col_all = col_all.reshape(n_col, panels, both, rank_most)
    col_u = col_all[:, :, :u_rows].transpose(1, 0, 2, 3).reshape(panels, tile_order, rank_most)
    col_v = col_all[:, :, u_rows:]

    weight = jnp.stack(
        [column_weight(u_scale[k], v_scale[k], ranks[k]) for k in range(panels)]
    )
    row_weight = lax.dynamic_slice_in_dim(weight, first_tile, per_row, 1)
    col_weight = lax.dynamic_index_in_dim(weight, column, 1, keepdims=False)

    half = v_rows // 2
    d_blocks = d_inverse.reshape(panels, 2, 2, n_col, half).transpose(1, 2, 3, 0, 4)[..., None]
    pairs = col_v.reshape(n_col, panels, half, 2, rank_most)
    even = pairs[..., 0, :].astype(jnp.float32)
    odd = pairs[..., 1, :].astype(jnp.float32)
    first = d_blocks[0, 0] * even + d_blocks[0, 1] * odd
    second = d_blocks[1, 0] * even + d_blocks[1, 1] * odd
    col_scaled = jnp.stack([first, second], axis=-2).reshape(col_v.shape).astype(jnp.bfloat16)

    inner = jnp.einsum("cikbr,ckbq->kirq", row_v, col_scaled, preferred_element_type=jnp.float32)
    core = (row_weight[:, :, :, None] * inner * col_weight[:, None, None, :]).astype(jnp.bfloat16)
    left = jnp.einsum("cikmr,kirq->kicmq", row_u, core, preferred_element_type=jnp.float32)
    left = left.astype(jnp.bfloat16)
    update = jnp.einsum("kicmq,knq->icmn", left, col_u, preferred_element_type=jnp.float32)
    return slab - update.reshape(slab.shape)


def solution(mesh):
    in_specs = (
        P("row", "col"),
        P(None, "row", "col", None),
        P(None, "row", "col", None),
        P(),
        P(),
        P(),
        P(),
    )
    out_specs = P("row", "col")
    return jax.shard_map(local, mesh=mesh, in_specs=in_specs, out_specs=out_specs, check_vma=False)
```

```python
import jax
import jax.numpy as jnp
from jax import lax
from jax.sharding import PartitionSpec as P


def column_weight(u_scale_k, v_scale_k, ranks_k):
    position = lax.broadcasted_iota(jnp.int32, u_scale_k.shape, 1)
    return jnp.where(position < ranks_k[:, None], u_scale_k * v_scale_k, jnp.float32(0.0))


def ring_gather(block, n_outer, n_inner, outer):
    n = n_outer if outer else n_inner

    def target(r, step):
        a, b = divmod(r, n_inner)
        if outer:
            return ((a + step) % n_outer) * n_inner + b
        return a * n_inner + (b + step) % n_inner

    pieces = [block]
    for d in range(1, n):
        perm = [(r, target(r, -d)) for r in range(n_outer * n_inner)]
        pieces.append(lax.ppermute(block, "row", perm))
    return jnp.stack(pieces)


def replicate_over_row(block, n_row):
    n_x = 4 if n_row % 4 == 0 else n_row
    n_z = n_row // n_x
    row = lax.axis_index("row")
    z, x = row // n_x, row % n_x
    by_z = ring_gather(block, n_z, n_x, outer=True)
    by_xz = ring_gather(by_z, n_z, n_x, outer=False)
    by_zx = jnp.roll(jnp.roll(by_xz, x, axis=0), z, axis=1).swapaxes(0, 1)
    return by_zx.reshape((n_row,) + block.shape)


def local(slab, u_codes, v_codes, u_scale, v_scale, ranks, d_inverse):
    panels, per_row, u_rows, rank_most = u_codes.shape
    v_rows = v_codes.shape[2]
    n_col = lax.axis_size("col")
    column = lax.axis_index("col")
    first_tile = lax.axis_index("row") * per_row
    tile_order = n_col * u_rows
    both = u_rows + v_rows

    shard = jnp.concatenate([u_codes, v_codes], axis=2).transpose(1, 0, 2, 3)

    row_all = lax.all_gather(shard, "col", axis=0, tiled=False)
    row_u = row_all[:, :, :, :u_rows]
    row_v = row_all[:, :, :, u_rows:]

    n_row = lax.axis_size("row")
    flat = shard.reshape(per_row * panels * both, rank_most)
    every_tile = replicate_over_row(flat, n_row)
    every_tile = every_tile.reshape(n_row * per_row, panels * both, rank_most)
    col_all = lax.all_to_all(every_tile, "col", 0, 0, tiled=True)
    col_all = col_all.reshape(n_col, panels, both, rank_most)
    col_u = col_all[:, :, :u_rows].transpose(1, 0, 2, 3).reshape(panels, tile_order, rank_most)
    col_v = col_all[:, :, u_rows:]

    weight = jnp.stack(
        [column_weight(u_scale[k], v_scale[k], ranks[k]) for k in range(panels)]
    )
    row_weight = lax.dynamic_slice_in_dim(weight, first_tile, per_row, 1)
    col_weight = lax.dynamic_index_in_dim(weight, column, 1, keepdims=False)

    half = v_rows // 2
    d_blocks = d_inverse.reshape(panels, 2, 2, n_col, half).transpose(1, 2, 3, 0, 4)[..., None]
    pairs = col_v.reshape(n_col, panels, half, 2, rank_most)
    even = pairs[..., 0, :].astype(jnp.float32)
    odd = pairs[..., 1, :].astype(jnp.float32)
    first = d_blocks[0, 0] * even + d_blocks[0, 1] * odd
    second = d_blocks[1, 0] * even + d_blocks[1, 1] * odd
    col_scaled = jnp.stack([first, second], axis=-2).reshape(col_v.shape).astype(jnp.bfloat16)

    inner = jnp.einsum("cikbr,ckbq->kirq", row_v, col_scaled, preferred_element_type=jnp.float32)
    core = (row_weight[:, :, :, None] * inner * col_weight[:, None, None, :]).astype(jnp.bfloat16)
    left = jnp.einsum("cikmr,kirq->kicmq", row_u, core, preferred_element_type=jnp.float32)
    left = left.astype(jnp.bfloat16)
    update = jnp.einsum("kicmq,knq->icmn", left, col_u, preferred_element_type=jnp.float32)
    return slab - update.reshape(slab.shape)


def solution(mesh):
    in_specs = (
        P("row", "col"),
        P(None, "row", "col", None),
        P(None, "row", "col", None),
        P(),
        P(),
        P(),
        P(),
    )
    out_specs = P("row", "col")
    return jax.shard_map(local, mesh=mesh, in_specs=in_specs, out_specs=out_specs, check_vma=False)
```

```python
import jax
import jax.numpy as jnp
from jax import lax
from jax.sharding import PartitionSpec as P


def column_weight(u_scale_k, v_scale_k, ranks_k):
    position = lax.broadcasted_iota(jnp.int32, u_scale_k.shape, 1)
    return jnp.where(position < ranks_k[:, None], u_scale_k * v_scale_k, jnp.float32(0.0))


def ring_gather(block, n_outer, n_inner, outer):
    n_all = n_outer * n_inner

    def target(r, step):
        a, b = divmod(r, n_inner)
        if outer:
            return ((a + step) % n_outer) * n_inner + b
        return a * n_inner + (b + step) % n_inner

    def shift(value, step):
        return lax.ppermute(value, "row", [(r, target(r, step)) for r in range(n_all)])

    from_behind = shift(block, 1)
    from_ahead = shift(block, -1)
    half = block.shape[-2] // 2
    far = jnp.concatenate(
        [shift(from_behind[..., :half, :], 1), shift(from_ahead[..., half:, :], -1)], axis=-2
    )
    return jnp.stack([block, from_ahead, far, from_behind])


def replicate_over_row(block, n_row):
    n_x = 4
    n_z = n_row // n_x
    row = lax.axis_index("row")
    z, x = row // n_x, row % n_x
    by_z = ring_gather(block, n_z, n_x, outer=True)
    by_xz = ring_gather(by_z, n_z, n_x, outer=False)
    by_zx = jnp.roll(jnp.roll(by_xz, x, axis=0), z, axis=1).swapaxes(0, 1)
    return by_zx.reshape((n_row,) + block.shape)


def local(slab, u_codes, v_codes, u_scale, v_scale, ranks, d_inverse):
    panels, per_row, u_rows, rank_most = u_codes.shape
    v_rows = v_codes.shape[2]
    n_col = lax.axis_size("col")
    column = lax.axis_index("col")
    first_tile = lax.axis_index("row") * per_row
    tile_order = n_col * u_rows
    both = u_rows + v_rows

    shard = jnp.concatenate([u_codes, v_codes], axis=2).transpose(1, 0, 2, 3)

    row_all = lax.all_gather(shard, "col", axis=0, tiled=False)
    row_u = row_all[:, :, :, :u_rows]
    row_v = row_all[:, :, :, u_rows:]

    n_row = lax.axis_size("row")
    flat = shard.reshape(per_row * panels * both, rank_most)
    every_tile = replicate_over_row(flat, n_row)
    every_tile = every_tile.reshape(n_row * per_row, panels * both, rank_most)
    col_all = lax.all_to_all(every_tile, "col", 0, 0, tiled=True)
    col_all = col_all.reshape(n_col, panels, both, rank_most)
    col_u = col_all[:, :, :u_rows].transpose(1, 0, 2, 3).reshape(panels, tile_order, rank_most)
    col_v = col_all[:, :, u_rows:]

    weight = jnp.stack(
        [column_weight(u_scale[k], v_scale[k], ranks[k]) for k in range(panels)]
    )
    row_weight = lax.dynamic_slice_in_dim(weight, first_tile, per_row, 1)
    col_weight = lax.dynamic_index_in_dim(weight, column, 1, keepdims=False)

    half = v_rows // 2
    d_blocks = d_inverse.reshape(panels, 2, 2, n_col, half).transpose(1, 2, 3, 0, 4)[..., None]
    pairs = col_v.reshape(n_col, panels, half, 2, rank_most)
    even = pairs[..., 0, :].astype(jnp.float32)
    odd = pairs[..., 1, :].astype(jnp.float32)
    first = d_blocks[0, 0] * even + d_blocks[0, 1] * odd
    second = d_blocks[1, 0] * even + d_blocks[1, 1] * odd
    col_scaled = jnp.stack([first, second], axis=-2).reshape(col_v.shape).astype(jnp.bfloat16)

    inner = jnp.einsum("cikbr,ckbq->kirq", row_v, col_scaled, preferred_element_type=jnp.float32)
    core = (row_weight[:, :, :, None] * inner * col_weight[:, None, None, :]).astype(jnp.bfloat16)
    left = jnp.einsum("cikmr,kirq->kicmq", row_u, core, preferred_element_type=jnp.float32)
    left = left.astype(jnp.bfloat16)
    update = jnp.einsum("kicmq,knq->icmn", left, col_u, preferred_element_type=jnp.float32)
    return slab - update.reshape(slab.shape)


def solution(mesh):
    in_specs = (
        P("row", "col"),
        P(None, "row", "col", None),
        P(None, "row", "col", None),
        P(),
        P(),
        P(),
        P(),
    )
    out_specs = P("row", "col")
    return jax.shard_map(local, mesh=mesh, in_specs=in_specs, out_specs=out_specs, check_vma=False)
```

```python
import jax
import jax.numpy as jnp
from jax import lax
from jax.sharding import PartitionSpec as P


def column_weight(u_scale_k, v_scale_k, ranks_k):
    position = lax.broadcasted_iota(jnp.int32, u_scale_k.shape, 1)
    return jnp.where(position < ranks_k[:, None], u_scale_k * v_scale_k, jnp.float32(0.0))


def ring_gather(block, n_outer, n_inner, outer, forward=True):
    n_all = n_outer * n_inner

    def target(r, step):
        a, b = divmod(r, n_inner)
        if outer:
            return ((a + step) % n_outer) * n_inner + b
        return a * n_inner + (b + step) % n_inner

    def shift(value, step):
        return lax.ppermute(value, "row", [(r, target(r, step)) for r in range(n_all)])

    if not forward:
        return jnp.stack([block] + [shift(block, -d) for d in range(1, 4)])
    from_behind = shift(block, 1)
    from_ahead = shift(block, -1)
    half = block.shape[-2] // 2
    far = jnp.concatenate(
        [shift(from_behind[..., :half, :], 1), shift(from_ahead[..., half:, :], -1)], axis=-2
    )
    return jnp.stack([block, from_ahead, far, from_behind])


def replicate_over_row(block, n_row):
    n_x = 4
    n_z = n_row // n_x
    row = lax.axis_index("row")
    z, x = row // n_x, row % n_x
    by_z = ring_gather(block, n_z, n_x, outer=True, forward=False)
    by_xz = ring_gather(by_z, n_z, n_x, outer=False)
    by_zx = jnp.roll(jnp.roll(by_xz, x, axis=0), z, axis=1).swapaxes(0, 1)
    return by_zx.reshape((n_row,) + block.shape)


def local(slab, u_codes, v_codes, u_scale, v_scale, ranks, d_inverse):
    panels, per_row, u_rows, rank_most = u_codes.shape
    v_rows = v_codes.shape[2]
    n_col = lax.axis_size("col")
    column = lax.axis_index("col")
    first_tile = lax.axis_index("row") * per_row
    tile_order = n_col * u_rows
    both = u_rows + v_rows

    shard = jnp.concatenate([u_codes, v_codes], axis=2).transpose(1, 0, 2, 3)

    row_all = lax.all_gather(shard, "col", axis=0, tiled=False)
    row_u = row_all[:, :, :, :u_rows]
    row_v = row_all[:, :, :, u_rows:]

    half = v_rows // 2
    d_own = lax.dynamic_slice_in_dim(d_inverse, column * half, half, 3)
    d_own = d_own.transpose(1, 2, 0, 3)[:, :, :, None, :, None]
    pairs = v_codes.reshape(panels, per_row, half, 2, rank_most)
    even = pairs[..., 0, :].astype(jnp.float32)
    odd = pairs[..., 1, :].astype(jnp.float32)
    first = d_own[0, 0] * even + d_own[0, 1] * odd
    second = d_own[1, 0] * even + d_own[1, 1] * odd
    v_scaled = jnp.stack([first, second], axis=-2).reshape(v_codes.shape).astype(jnp.bfloat16)
    col_shard = jnp.concatenate([u_codes, v_scaled], axis=2).transpose(1, 0, 2, 3)

    n_row = lax.axis_size("row")
    flat = col_shard.reshape(per_row * panels * both, rank_most)
    every_tile = replicate_over_row(flat, n_row)
    every_tile = every_tile.reshape(n_row * per_row, panels * both, rank_most)
    col_all = lax.all_to_all(every_tile, "col", 0, 0, tiled=True)
    col_all = col_all.reshape(n_col, panels, both, rank_most)
    col_u = col_all[:, :, :u_rows].transpose(1, 0, 2, 3).reshape(panels, tile_order, rank_most)
    col_v = col_all[:, :, u_rows:]

    weight = jnp.stack(
        [column_weight(u_scale[k], v_scale[k], ranks[k]) for k in range(panels)]
    )
    row_weight = lax.dynamic_slice_in_dim(weight, first_tile, per_row, 1)
    col_weight = lax.dynamic_index_in_dim(weight, column, 1, keepdims=False)

    col_scaled = col_v
    inner = jnp.einsum("cikbr,ckbq->kirq", row_v, col_scaled, preferred_element_type=jnp.float32)
    core = (row_weight[:, :, :, None] * inner * col_weight[:, None, None, :]).astype(jnp.bfloat16)
    left = jnp.einsum("cikmr,kirq->kicmq", row_u, core, preferred_element_type=jnp.float32)
    left = left.astype(jnp.bfloat16)
    update = jnp.einsum("kicmq,knq->icmn", left, col_u, preferred_element_type=jnp.float32)
    return slab - update.reshape(slab.shape)


def solution(mesh):
    in_specs = (
        P("row", "col"),
        P(None, "row", "col", None),
        P(None, "row", "col", None),
        P(),
        P(),
        P(),
        P(),
    )
    out_specs = P("row", "col")
    return jax.shard_map(local, mesh=mesh, in_specs=in_specs, out_specs=out_specs, check_vma=False)
```

```python
import jax
import jax.numpy as jnp
from jax import lax
from jax.sharding import PartitionSpec as P


def column_weight(u_scale_k, v_scale_k, ranks_k):
    position = lax.broadcasted_iota(jnp.int32, u_scale_k.shape, 1)
    return jnp.where(position < ranks_k[:, None], u_scale_k * v_scale_k, jnp.float32(0.0))


def ring_gather(block, n_outer, n_inner, outer, forward=True):
    n_all = n_outer * n_inner

    def target(r, step):
        a, b = divmod(r, n_inner)
        if outer:
            return ((a + step) % n_outer) * n_inner + b
        return a * n_inner + (b + step) % n_inner

    def shift(value, step):
        return lax.ppermute(value, "row", [(r, target(r, step)) for r in range(n_all)])

    if not forward:
        return jnp.stack([block] + [shift(block, -d) for d in range(1, 4)])
    from_behind = shift(block, 1)
    from_ahead = shift(block, -1)
    half = block.shape[-2] // 2
    far = jnp.concatenate(
        [shift(from_behind[..., :half, :], 1), shift(from_ahead[..., half:, :], -1)], axis=-2
    )
    return jnp.stack([block, from_ahead, far, from_behind])


def replicate_over_row(block, n_row):
    n_x = 4
    n_z = n_row // n_x
    row = lax.axis_index("row")
    z, x = row // n_x, row % n_x
    by_z = ring_gather(block, n_z, n_x, outer=True)
    by_xz = ring_gather(by_z, n_z, n_x, outer=False)
    by_zx = jnp.roll(jnp.roll(by_xz, x, axis=0), z, axis=1).swapaxes(0, 1)
    return by_zx.reshape((n_row,) + block.shape)


def local(slab, u_codes, v_codes, u_scale, v_scale, ranks, d_inverse):
    panels, per_row, u_rows, rank_most = u_codes.shape
    v_rows = v_codes.shape[2]
    n_col = lax.axis_size("col")
    column = lax.axis_index("col")
    first_tile = lax.axis_index("row") * per_row
    tile_order = n_col * u_rows
    both = u_rows + v_rows

    shard = jnp.concatenate([u_codes, v_codes], axis=2).transpose(1, 0, 2, 3)

    row_all = lax.all_gather(shard, "col", axis=0, tiled=False)
    row_u = row_all[:, :, :, :u_rows]
    row_v = row_all[:, :, :, u_rows:]

    half = v_rows // 2
    d_own = lax.dynamic_slice_in_dim(d_inverse, column * half, half, 3)
    d_own = d_own.transpose(1, 2, 0, 3)[:, :, :, None, :, None]
    pairs = v_codes.reshape(panels, per_row, half, 2, rank_most)
    even = pairs[..., 0, :].astype(jnp.float32)
    odd = pairs[..., 1, :].astype(jnp.float32)
    first = d_own[0, 0] * even + d_own[0, 1] * odd
    second = d_own[1, 0] * even + d_own[1, 1] * odd
    v_scaled = jnp.stack([first, second], axis=-2).reshape(v_codes.shape).astype(jnp.bfloat16)
    col_shard = jnp.concatenate([u_codes, v_scaled], axis=2).transpose(1, 0, 2, 3)

    n_row = lax.axis_size("row")
    flat = col_shard.reshape(per_row * panels * both, rank_most)
    every_tile = replicate_over_row(flat, n_row)
    every_tile = every_tile.reshape(n_row * per_row, panels * both, rank_most)
    col_all = lax.all_to_all(every_tile, "col", 0, 0, tiled=True)
    col_all = col_all.reshape(n_col, panels, both, rank_most)
    col_u = col_all[:, :, :u_rows].transpose(1, 0, 2, 3).reshape(panels, tile_order, rank_most)
    col_v = col_all[:, :, u_rows:]

    weight = jnp.stack(
        [column_weight(u_scale[k], v_scale[k], ranks[k]) for k in range(panels)]
    )
    row_weight = lax.dynamic_slice_in_dim(weight, first_tile, per_row, 1)
    col_weight = lax.dynamic_index_in_dim(weight, column, 1, keepdims=False)

    col_scaled = col_v
    inner = jnp.einsum("cikbr,ckbq->kirq", row_v, col_scaled, preferred_element_type=jnp.float32)
    core = (row_weight[:, :, :, None] * inner * col_weight[:, None, None, :]).astype(jnp.bfloat16)
    left = jnp.einsum("cikmr,kirq->kicmq", row_u, core, preferred_element_type=jnp.float32)
    left = left.astype(jnp.bfloat16)
    update = jnp.einsum("kicmq,knq->icmn", left, col_u, preferred_element_type=jnp.float32)
    return slab - update.reshape(slab.shape)


def solution(mesh):
    in_specs = (
        P("row", "col"),
        P(None, "row", "col", None),
        P(None, "row", "col", None),
        P(),
        P(),
        P(),
        P(),
    )
    out_specs = P("row", "col")
    return jax.shard_map(local, mesh=mesh, in_specs=in_specs, out_specs=out_specs, check_vma=False)
```

```python
import jax
import jax.numpy as jnp
from jax import lax
from jax.sharding import Mesh, PartitionSpec as P


def column_weight(u_scale_k, v_scale_k, ranks_k):
    position = lax.broadcasted_iota(jnp.int32, u_scale_k.shape, 1)
    return jnp.where(position < ranks_k[:, None], u_scale_k * v_scale_k, jnp.float32(0.0))


def ring_gather(block, n_outer, n_inner, outer, forward=True):
    n_all = n_outer * n_inner

    def target(r, step):
        a, b = divmod(r, n_inner)
        if outer:
            return ((a + step) % n_outer) * n_inner + b
        return a * n_inner + (b + step) % n_inner

    def shift(value, step):
        return lax.ppermute(value, "row", [(r, target(r, step)) for r in range(n_all)])

    if not forward:
        return jnp.stack([block] + [shift(block, -d) for d in range(1, 4)])
    from_behind = shift(block, 1)
    from_ahead = shift(block, -1)
    half = block.shape[-2] // 2
    far = jnp.concatenate(
        [shift(from_behind[..., :half, :], 1), shift(from_ahead[..., half:, :], -1)], axis=-2
    )
    return jnp.stack([block, from_ahead, far, from_behind])


def replicate_over_row(block, n_row):
    n_x = 4
    n_z = n_row // n_x
    row = lax.axis_index("row")
    z, x = row // n_x, row % n_x
    by_z = ring_gather(block, n_z, n_x, outer=True)
    by_xz = ring_gather(by_z, n_z, n_x, outer=False)
    by_zx = jnp.roll(jnp.roll(by_xz, x, axis=0), z, axis=1).swapaxes(0, 1)
    return by_zx.reshape((n_row,) + block.shape)


def local(slab, u_codes, v_codes, u_scale, v_scale, ranks, d_inverse):
    panels, per_row, u_rows, rank_most = u_codes.shape
    v_rows = v_codes.shape[2]
    n_core = lax.axis_size("core")
    n_col = lax.axis_size("yz") * n_core
    core = lax.axis_index("core")
    column = lax.axis_index("yz") * n_core + core
    first_tile = lax.axis_index("row") * per_row
    tile_order = n_col * u_rows
    both = u_rows + v_rows

    shard = jnp.concatenate([u_codes, v_codes], axis=2).transpose(1, 0, 2, 3)

    mine = lax.all_gather(shard, "yz", axis=0, tiled=False)
    other = lax.ppermute(mine, "core", [(0, 1), (1, 0)])
    first = jnp.where(core == 0, mine, other)
    second = jnp.where(core == 0, other, mine)
    row_all = jnp.stack([first, second], axis=1).reshape((n_col,) + shard.shape)
    row_u = row_all[:, :, :, :u_rows]
    row_v = row_all[:, :, :, u_rows:]

    half = v_rows // 2
    d_own = lax.dynamic_slice_in_dim(d_inverse, column * half, half, 3)
    d_own = d_own.transpose(1, 2, 0, 3)[:, :, :, None, :, None]
    pairs = v_codes.reshape(panels, per_row, half, 2, rank_most)
    even = pairs[..., 0, :].astype(jnp.float32)
    odd = pairs[..., 1, :].astype(jnp.float32)
    first = d_own[0, 0] * even + d_own[0, 1] * odd
    second = d_own[1, 0] * even + d_own[1, 1] * odd
    v_scaled = jnp.stack([first, second], axis=-2).reshape(v_codes.shape).astype(jnp.bfloat16)
    col_shard = jnp.concatenate([u_codes, v_scaled], axis=2).transpose(1, 0, 2, 3)

    n_row = lax.axis_size("row")
    flat = col_shard.reshape(per_row * panels * both, rank_most)
    every_tile = replicate_over_row(flat, n_row)
    every_tile = every_tile.reshape(n_row * per_row, panels * both, rank_most)
    col_all = lax.all_to_all(every_tile, ("yz", "core"), 0, 0, tiled=True)
    col_all = col_all.reshape(n_col, panels, both, rank_most)
    col_u = col_all[:, :, :u_rows].transpose(1, 0, 2, 3).reshape(panels, tile_order, rank_most)
    col_v = col_all[:, :, u_rows:]

    weight = jnp.stack(
        [column_weight(u_scale[k], v_scale[k], ranks[k]) for k in range(panels)]
    )
    row_weight = lax.dynamic_slice_in_dim(weight, first_tile, per_row, 1)
    col_weight = lax.dynamic_index_in_dim(weight, column, 1, keepdims=False)

    col_scaled = col_v
    inner = jnp.einsum("cikbr,ckbq->kirq", row_v, col_scaled, preferred_element_type=jnp.float32)
    core = (row_weight[:, :, :, None] * inner * col_weight[:, None, None, :]).astype(jnp.bfloat16)
    left = jnp.einsum("cikmr,kirq->kicmq", row_u, core, preferred_element_type=jnp.float32)
    left = left.astype(jnp.bfloat16)
    update = jnp.einsum("kicmq,knq->icmn", left, col_u, preferred_element_type=jnp.float32)
    return slab - update.reshape(slab.shape)


def solution(mesh):
    n_row, n_col = mesh.devices.shape
    split = Mesh(mesh.devices.reshape(n_row, n_col // 2, 2), ("row", "yz", "core"))
    cols = ("yz", "core")
    in_specs = (
        P("row", cols),
        P(None, "row", cols, None),
        P(None, "row", cols, None),
        P(),
        P(),
        P(),
        P(),
    )
    out_specs = P("row", cols)
    return jax.shard_map(local, mesh=split, in_specs=in_specs, out_specs=out_specs, check_vma=False)
```

```python
import jax
import jax.numpy as jnp
from jax import lax
from jax.sharding import PartitionSpec as P


def column_weight(u_scale_k, v_scale_k, ranks_k):
    position = lax.broadcasted_iota(jnp.int32, u_scale_k.shape, 1)
    return jnp.where(position < ranks_k[:, None], u_scale_k * v_scale_k, jnp.float32(0.0))


def ring_gather(block, n_outer, n_inner, outer, forward=True):
    n_all = n_outer * n_inner

    def target(r, step):
        a, b = divmod(r, n_inner)
        if outer:
            return ((a + step) % n_outer) * n_inner + b
        return a * n_inner + (b + step) % n_inner

    def shift(value, step):
        return lax.ppermute(value, "row", [(r, target(r, step)) for r in range(n_all)])

    if not forward:
        return jnp.stack([block] + [shift(block, -d) for d in range(1, 4)])
    from_behind = shift(block, 1)
    from_ahead = shift(block, -1)
    half = block.shape[-2] // 2
    far = jnp.concatenate(
        [shift(from_behind[..., :half, :], 1), shift(from_ahead[..., half:, :], -1)], axis=-2
    )
    return jnp.stack([block, from_ahead, far, from_behind])


def replicate_over_row(block, n_row):
    n_x = 4
    n_z = n_row // n_x
    row = lax.axis_index("row")
    z, x = row // n_x, row % n_x
    by_z = ring_gather(block, n_z, n_x, outer=True)
    by_xz = ring_gather(by_z, n_z, n_x, outer=False)
    by_zx = jnp.roll(jnp.roll(by_xz, x, axis=0), z, axis=1).swapaxes(0, 1)
    return by_zx.reshape((n_row,) + block.shape)


def local(slab, u_codes, v_codes, u_scale, v_scale, ranks, d_inverse):
    panels, per_row, u_rows, rank_most = u_codes.shape
    v_rows = v_codes.shape[2]
    n_col = lax.axis_size("col")
    column = lax.axis_index("col")
    first_tile = lax.axis_index("row") * per_row
    tile_order = n_col * u_rows
    both = u_rows + v_rows

    shard = jnp.concatenate([u_codes, v_codes], axis=2).transpose(1, 0, 2, 3)

    row_all = lax.all_gather(shard, "col", axis=0, tiled=False)
    row_u = row_all[:, :, :, :u_rows]
    row_v = row_all[:, :, :, u_rows:]

    half = v_rows // 2
    d_own = lax.dynamic_slice_in_dim(d_inverse, column * half, half, 3)
    d_own = jnp.repeat(d_own, 2, axis=3)
    parity = lax.broadcasted_iota(jnp.int32, (v_rows,), 0) % 2
    even_row = parity == 0
    own_scale = jnp.where(even_row, d_own[:, 0, 0], d_own[:, 1, 1])
    partner_scale = jnp.where(even_row, d_own[:, 0, 1], d_own[:, 1, 0])
    codes = v_codes.astype(jnp.float32)
    partner = jnp.where(
        even_row[:, None], jnp.roll(codes, -1, axis=2), jnp.roll(codes, 1, axis=2)
    )
    v_scaled = (
        own_scale[:, None, :, None] * codes + partner_scale[:, None, :, None] * partner
    ).astype(jnp.bfloat16)
    col_shard = jnp.concatenate([u_codes, v_scaled], axis=2).transpose(1, 0, 2, 3)

    n_row = lax.axis_size("row")
    flat = col_shard.reshape(per_row * panels * both, rank_most)
    every_tile = replicate_over_row(flat, n_row)
    every_tile = every_tile.reshape(n_row * per_row, panels * both, rank_most)
    col_all = lax.all_to_all(every_tile, "col", 0, 0, tiled=True)
    col_all = col_all.reshape(n_col, panels, both, rank_most)
    col_u = col_all[:, :, :u_rows].transpose(1, 0, 2, 3).reshape(panels, tile_order, rank_most)
    col_v = col_all[:, :, u_rows:]

    weight = jnp.stack(
        [column_weight(u_scale[k], v_scale[k], ranks[k]) for k in range(panels)]
    )
    row_weight = lax.dynamic_slice_in_dim(weight, first_tile, per_row, 1)
    col_weight = lax.dynamic_index_in_dim(weight, column, 1, keepdims=False)

    col_scaled = col_v
    inner = jnp.einsum("cikbr,ckbq->kirq", row_v, col_scaled, preferred_element_type=jnp.float32)
    core = (row_weight[:, :, :, None] * inner * col_weight[:, None, None, :]).astype(jnp.bfloat16)
    left = jnp.einsum("cikmr,kirq->kicmq", row_u, core, preferred_element_type=jnp.float32)
    left = left.astype(jnp.bfloat16)
    update = jnp.einsum("kicmq,knq->icmn", left, col_u, preferred_element_type=jnp.float32)
    return slab - update.reshape(slab.shape)


def solution(mesh):
    in_specs = (
        P("row", "col"),
        P(None, "row", "col", None),
        P(None, "row", "col", None),
        P(),
        P(),
        P(),
        P(),
    )
    out_specs = P("row", "col")
    return jax.shard_map(local, mesh=mesh, in_specs=in_specs, out_specs=out_specs, check_vma=False)
```

```python
import jax
import jax.numpy as jnp
from jax import lax
from jax.sharding import PartitionSpec as P


def column_weight(u_scale_k, v_scale_k, ranks_k):
    position = lax.broadcasted_iota(jnp.int32, u_scale_k.shape, 1)
    return jnp.where(position < ranks_k[:, None], u_scale_k * v_scale_k, jnp.float32(0.0))


def ring_gather(block, n_outer, n_inner, outer, forward=True):
    n_all = n_outer * n_inner

    def target(r, step):
        a, b = divmod(r, n_inner)
        if outer:
            return ((a + step) % n_outer) * n_inner + b
        return a * n_inner + (b + step) % n_inner

    def shift(value, step):
        return lax.ppermute(value, "row", [(r, target(r, step)) for r in range(n_all)])

    if not forward:
        return jnp.stack([block] + [shift(block, -d) for d in range(1, 4)])
    from_behind = shift(block, 1)
    from_ahead = shift(block, -1)
    if forward == "whole":
        return jnp.stack([block, from_ahead, shift(from_behind, 1), from_behind])
    half = block.shape[-2] // 2
    far = jnp.concatenate(
        [shift(from_behind[..., :half, :], 1), shift(from_ahead[..., half:, :], -1)], axis=-2
    )
    return jnp.stack([block, from_ahead, far, from_behind])


def replicate_over_row(block, n_row):
    n_x = 4
    n_z = n_row // n_x
    row = lax.axis_index("row")
    z, x = row // n_x, row % n_x
    by_z = ring_gather(block, n_z, n_x, outer=True, forward="whole")
    by_xz = ring_gather(by_z, n_z, n_x, outer=False)
    by_zx = jnp.roll(jnp.roll(by_xz, x, axis=0), z, axis=1).swapaxes(0, 1)
    return by_zx.reshape((n_row,) + block.shape)


def local(slab, u_codes, v_codes, u_scale, v_scale, ranks, d_inverse):
    panels, per_row, u_rows, rank_most = u_codes.shape
    v_rows = v_codes.shape[2]
    n_col = lax.axis_size("col")
    column = lax.axis_index("col")
    first_tile = lax.axis_index("row") * per_row
    tile_order = n_col * u_rows
    both = u_rows + v_rows

    shard = jnp.concatenate([u_codes, v_codes], axis=2).transpose(1, 0, 2, 3)

    row_all = lax.all_gather(shard, "col", axis=0, tiled=False)
    row_u = row_all[:, :, :, :u_rows]
    row_v = row_all[:, :, :, u_rows:]

    half = v_rows // 2
    d_own = lax.dynamic_slice_in_dim(d_inverse, column * half, half, 3)
    d_own = jnp.repeat(d_own, 2, axis=3)
    parity = lax.broadcasted_iota(jnp.int32, (v_rows,), 0) % 2
    even_row = parity == 0
    own_scale = jnp.where(even_row, d_own[:, 0, 0], d_own[:, 1, 1])
    partner_scale = jnp.where(even_row, d_own[:, 0, 1], d_own[:, 1, 0])
    codes = v_codes.astype(jnp.float32)
    partner = jnp.where(
        even_row[:, None], jnp.roll(codes, -1, axis=2), jnp.roll(codes, 1, axis=2)
    )
    v_scaled = (
        own_scale[:, None, :, None] * codes + partner_scale[:, None, :, None] * partner
    ).astype(jnp.bfloat16)
    col_shard = jnp.concatenate([u_codes, v_scaled], axis=2).transpose(1, 0, 2, 3)

    n_row = lax.axis_size("row")
    flat = col_shard.reshape(per_row * panels * both, rank_most)
    every_tile = replicate_over_row(flat, n_row)
    every_tile = every_tile.reshape(n_row * per_row, panels * both, rank_most)
    col_all = lax.all_to_all(every_tile, "col", 0, 0, tiled=True)
    col_all = col_all.reshape(n_col, panels, both, rank_most)
    col_u = col_all[:, :, :u_rows].transpose(1, 0, 2, 3).reshape(panels, tile_order, rank_most)
    col_v = col_all[:, :, u_rows:]

    weight = jnp.stack(
        [column_weight(u_scale[k], v_scale[k], ranks[k]) for k in range(panels)]
    )
    row_weight = lax.dynamic_slice_in_dim(weight, first_tile, per_row, 1)
    col_weight = lax.dynamic_index_in_dim(weight, column, 1, keepdims=False)

    col_scaled = col_v
    inner = jnp.einsum("cikbr,ckbq->kirq", row_v, col_scaled, preferred_element_type=jnp.float32)
    core = (row_weight[:, :, :, None] * inner * col_weight[:, None, None, :]).astype(jnp.bfloat16)
    left = jnp.einsum("cikmr,kirq->kicmq", row_u, core, preferred_element_type=jnp.float32)
    left = left.astype(jnp.bfloat16)
    update = jnp.einsum("kicmq,knq->icmn", left, col_u, preferred_element_type=jnp.float32)
    return slab - update.reshape(slab.shape)


def solution(mesh):
    in_specs = (
        P("row", "col"),
        P(None, "row", "col", None),
        P(None, "row", "col", None),
        P(),
        P(),
        P(),
        P(),
    )
    out_specs = P("row", "col")
    return jax.shard_map(local, mesh=mesh, in_specs=in_specs, out_specs=out_specs, check_vma=False)
```

```python
import jax
import jax.numpy as jnp
from jax import lax
from jax.sharding import PartitionSpec as P


def column_weight(u_scale_k, v_scale_k, ranks_k):
    position = lax.broadcasted_iota(jnp.int32, u_scale_k.shape, 1)
    return jnp.where(position < ranks_k[:, None], u_scale_k * v_scale_k, jnp.float32(0.0))


def ring_gather(block, n_outer, n_inner, outer, forward=True):
    n_all = n_outer * n_inner

    def target(r, step):
        a, b = divmod(r, n_inner)
        if outer:
            return ((a + step) % n_outer) * n_inner + b
        return a * n_inner + (b + step) % n_inner

    def shift(value, step):
        return lax.ppermute(value, "row", [(r, target(r, step)) for r in range(n_all)])

    if not forward:
        return jnp.stack([block] + [shift(block, -d) for d in range(1, 4)])
    from_behind = shift(block, 1)
    from_ahead = shift(block, -1)
    half = block.shape[-2] // 2
    far = jnp.concatenate(
        [shift(from_behind[..., :half, :], 1), shift(from_ahead[..., half:, :], -1)], axis=-2
    )
    return jnp.stack([block, from_ahead, far, from_behind])


def replicate_over_row(block, n_row):
    n_x = 4
    n_z = n_row // n_x
    row = lax.axis_index("row")
    z, x = row // n_x, row % n_x
    by_z = ring_gather(block, n_z, n_x, outer=True)
    by_xz = ring_gather(by_z, n_z, n_x, outer=False)
    by_zx = jnp.roll(jnp.roll(by_xz, x, axis=0), z, axis=1).swapaxes(0, 1)
    return by_zx.reshape((n_row,) + block.shape)


def local(slab, u_codes, v_codes, u_scale, v_scale, ranks, d_inverse):
    panels, per_row, u_rows, rank_most = u_codes.shape
    v_rows = v_codes.shape[2]
    n_col = lax.axis_size("col")
    column = lax.axis_index("col")
    first_tile = lax.axis_index("row") * per_row
    tile_order = n_col * u_rows
    both = u_rows + v_rows

    shard = jnp.concatenate([u_codes, v_codes], axis=2)

    row_all = lax.all_gather(shard, "col", axis=0, tiled=False)
    row_u = row_all[:, :, :, :u_rows]
    row_v = row_all[:, :, :, u_rows:]

    half = v_rows // 2
    d_own = lax.dynamic_slice_in_dim(d_inverse, column * half, half, 3)
    d_own = jnp.repeat(d_own, 2, axis=3)
    parity = lax.broadcasted_iota(jnp.int32, (v_rows,), 0) % 2
    even_row = parity == 0
    own_scale = jnp.where(even_row, d_own[:, 0, 0], d_own[:, 1, 1])
    partner_scale = jnp.where(even_row, d_own[:, 0, 1], d_own[:, 1, 0])
    codes = v_codes.astype(jnp.float32)
    partner = jnp.where(
        even_row[:, None], jnp.roll(codes, -1, axis=2), jnp.roll(codes, 1, axis=2)
    )
    v_scaled = (
        own_scale[:, None, :, None] * codes + partner_scale[:, None, :, None] * partner
    ).astype(jnp.bfloat16)
    col_shard = jnp.concatenate([u_codes, v_scaled], axis=2).transpose(1, 0, 2, 3)

    n_row = lax.axis_size("row")
    flat = col_shard.reshape(per_row * panels * both, rank_most)
    every_tile = replicate_over_row(flat, n_row)
    every_tile = every_tile.reshape(n_row * per_row, panels * both, rank_most)
    col_all = lax.all_to_all(every_tile, "col", 0, 0, tiled=True)
    col_all = col_all.reshape(n_col, panels, both, rank_most)
    col_u = col_all[:, :, :u_rows].transpose(1, 0, 2, 3).reshape(panels, tile_order, rank_most)
    col_v = col_all[:, :, u_rows:]

    weight = jnp.stack(
        [column_weight(u_scale[k], v_scale[k], ranks[k]) for k in range(panels)]
    )
    row_weight = lax.dynamic_slice_in_dim(weight, first_tile, per_row, 1)
    col_weight = lax.dynamic_index_in_dim(weight, column, 1, keepdims=False)

    col_scaled = col_v
    inner = jnp.einsum("ckibr,ckbq->kirq", row_v, col_scaled, preferred_element_type=jnp.float32)
    core = (row_weight[:, :, :, None] * inner * col_weight[:, None, None, :]).astype(jnp.bfloat16)
    left = jnp.einsum("ckimr,kirq->kicmq", row_u, core, preferred_element_type=jnp.float32)
    left = left.astype(jnp.bfloat16)
    update = jnp.einsum("kicmq,knq->icmn", left, col_u, preferred_element_type=jnp.float32)
    return slab - update.reshape(slab.shape)


def solution(mesh):
    in_specs = (
        P("row", "col"),
        P(None, "row", "col", None),
        P(None, "row", "col", None),
        P(),
        P(),
        P(),
        P(),
    )
    out_specs = P("row", "col")
    return jax.shard_map(local, mesh=mesh, in_specs=in_specs, out_specs=out_specs, check_vma=False)
```

```python
import jax
import jax.numpy as jnp
from jax import lax
from jax.sharding import PartitionSpec as P


def column_weight(u_scale_k, v_scale_k, ranks_k):
    position = lax.broadcasted_iota(jnp.int32, u_scale_k.shape, 1)
    return jnp.where(position < ranks_k[:, None], u_scale_k * v_scale_k, jnp.float32(0.0))


def ring_gather(block, n_outer, n_inner, outer, forward=True):
    n_all = n_outer * n_inner

    def target(r, step):
        a, b = divmod(r, n_inner)
        if outer:
            return ((a + step) % n_outer) * n_inner + b
        return a * n_inner + (b + step) % n_inner

    def shift(value, step):
        return lax.ppermute(value, "row", [(r, target(r, step)) for r in range(n_all)])

    if not forward:
        return [block] + [shift(block, -d) for d in range(1, 4)]
    from_behind = shift(block, 1)
    from_ahead = shift(block, -1)
    half = block.shape[-2] // 2
    far = jnp.concatenate(
        [shift(from_behind[..., :half, :], 1), shift(from_ahead[..., half:, :], -1)], axis=-2
    )
    return [block, from_ahead, far, from_behind]


def replicate_over_row(block, n_row):
    n_x = 4
    n_z = n_row // n_x
    row = lax.axis_index("row")
    z, x = row // n_x, row % n_x
    by_z = jnp.stack(ring_gather(block, n_z, n_x, outer=True))
    by_z = jnp.roll(by_z, z, axis=0)
    by_zx = jnp.zeros((n_z, n_x) + block.shape, block.dtype)
    for d, piece in enumerate(ring_gather(by_z, n_z, n_x, outer=False)):
        by_zx = lax.dynamic_update_slice(by_zx, piece[:, None], (0, (x + d) % n_x, 0, 0))
    return by_zx.reshape((n_row,) + block.shape)


def local(slab, u_codes, v_codes, u_scale, v_scale, ranks, d_inverse):
    panels, per_row, u_rows, rank_most = u_codes.shape
    v_rows = v_codes.shape[2]
    n_col = lax.axis_size("col")
    column = lax.axis_index("col")
    first_tile = lax.axis_index("row") * per_row
    tile_order = n_col * u_rows
    both = u_rows + v_rows

    shard = jnp.concatenate([u_codes, v_codes], axis=2).transpose(1, 0, 2, 3)

    row_all = lax.all_gather(shard, "col", axis=0, tiled=False)
    row_u = row_all[:, :, :, :u_rows]
    row_v = row_all[:, :, :, u_rows:]

    half = v_rows // 2
    d_own = lax.dynamic_slice_in_dim(d_inverse, column * half, half, 3)
    d_own = jnp.repeat(d_own, 2, axis=3)
    parity = lax.broadcasted_iota(jnp.int32, (v_rows,), 0) % 2
    even_row = parity == 0
    own_scale = jnp.where(even_row, d_own[:, 0, 0], d_own[:, 1, 1])
    partner_scale = jnp.where(even_row, d_own[:, 0, 1], d_own[:, 1, 0])
    codes = v_codes.astype(jnp.float32)
    partner = jnp.where(
        even_row[:, None], jnp.roll(codes, -1, axis=2), jnp.roll(codes, 1, axis=2)
    )
    v_scaled = (
        own_scale[:, None, :, None] * codes + partner_scale[:, None, :, None] * partner
    ).astype(jnp.bfloat16)
    col_shard = jnp.concatenate([u_codes, v_scaled], axis=2).transpose(1, 0, 2, 3)

    n_row = lax.axis_size("row")
    flat = col_shard.reshape(per_row * panels * both, rank_most)
    every_tile = replicate_over_row(flat, n_row)
    every_tile = every_tile.reshape(n_row * per_row, panels * both, rank_most)
    col_all = lax.all_to_all(every_tile, "col", 0, 0, tiled=True)
    col_all = col_all.reshape(n_col, panels, both, rank_most)
    col_u = col_all[:, :, :u_rows].transpose(1, 0, 2, 3).reshape(panels, tile_order, rank_most)
    col_v = col_all[:, :, u_rows:]

    weight = jnp.stack(
        [column_weight(u_scale[k], v_scale[k], ranks[k]) for k in range(panels)]
    )
    row_weight = lax.dynamic_slice_in_dim(weight, first_tile, per_row, 1)
    col_weight = lax.dynamic_index_in_dim(weight, column, 1, keepdims=False)

    col_scaled = col_v
    inner = jnp.einsum("cikbr,ckbq->kirq", row_v, col_scaled, preferred_element_type=jnp.float32)
    core = (row_weight[:, :, :, None] * inner * col_weight[:, None, None, :]).astype(jnp.bfloat16)
    left = jnp.einsum("cikmr,kirq->kicmq", row_u, core, preferred_element_type=jnp.float32)
    left = left.astype(jnp.bfloat16)
    update = jnp.einsum("kicmq,knq->icmn", left, col_u, preferred_element_type=jnp.float32)
    return slab - update.reshape(slab.shape)


def solution(mesh):
    in_specs = (
        P("row", "col"),
        P(None, "row", "col", None),
        P(None, "row", "col", None),
        P(),
        P(),
        P(),
        P(),
    )
    out_specs = P("row", "col")
    return jax.shard_map(local, mesh=mesh, in_specs=in_specs, out_specs=out_specs, check_vma=False)
```
